256 devices in a mesh: dp: 4 (over y), expert: 64 (over x, z, core).
Axes of the slice: x: 4, y: 4, z: 8, core: 2. Of those that a mesh axis runs over, the one named last changes fastest.
Arguments:
- hidden: bfloat16 [32768, 2, 1024], P(('dp', 'expert')), may hold values from -6 to 6
- routes: int32 [32768, 2], P(('dp', 'expert')), may hold values from 0 to 63, all different within a row; in each aligned block of 128 rows (0 to 127, 128 to 255, ...) at most 8 rows name the same one
- gates: float32 [32768, 2], P(('dp', 'expert')), may hold values from 0.1 to 1
- cotangent: bfloat16 [32768, 7168], P(('dp', 'expert')), may hold values from -1.796875 to 1.796875
- weight: bfloat16 [64, 1024, 7168], P('expert', None, 'dp'), may hold values from -0.0625 to 0.0625
Outputs:
- grad_hidden: bfloat16 [32768, 2, 1024], P(('dp', 'expert'))
- grad_gates: float32 [32768, 2], P(('dp', 'expert'))
- grad_weight: bfloat16 [64, 1024, 7168], P('expert', None, 'dp')
The draws below stay inside these ranges and needn't reach their ends.
Inputs may be any that keep to these rules, and one draw needn't show every extreme that they name: `routes`: each row names 2 different experts; in each aligned block of 128 rows (the rows of one device) no expert is named by more than 8 rows, a bound that some block reaches.
All inputs are finite; a program needn't handle non-finite values.
Results may differ from the reference program's by a relative error of at most 0.0049.
Values may be sent and summed in bfloat16 or wider, within the bound.
No kernel may reach another device: no remote copies, remote signals or barrier semaphores. Data moves between devices by JAX's collectives and lax.ppermute only.
A program may use at most 128 MiB of HBM per device.

```python
import math
import jax
import jax.numpy as jnp
import numpy as np
from jax import lax

D = 7168
FF = 1024
TOP = 2
TOK_DEV = 128
EXPERTS = 64
MOST = 8
TOKENS = 32768
N_DP = 4
N_EXPERT = 64


def level_of(own_key, shape, shards, least, high):
    loudness, own = 1.0, jax.random.fold_in(own_key, 6)
    for position, shards_of in shards:
        draws = jnp.exp(jax.random.uniform(jax.random.fold_in(own, position), (shards_of,), jnp.float32, least / len(shards), high / len(shards)))
        loudness = loudness * jnp.repeat(draws, shape[position] // shards_of).reshape([-1 if axis == position else 1 for axis in range(len(shape))])
    return loudness


def routed_block(rng, own, number, rows, amount, top, most, lean):
    order = jax.random.permutation(rng, amount)
    heavy_load, usual = portions_of(amount, rows * top, most, lean, True), portions_of(amount, rows * top, most, lean, False)
    places = jnp.arange(amount)

    def named(tallies, turn):
        used = int((tallies > 0).sum())
        fixed = max(1, used // 4)
        shifted = fixed + (places - fixed + turn * (used - fixed)) % max(1, amount - fixed)
        return jnp.zeros((amount,), jnp.int32).at[order[jnp.where(places < fixed, places, shifted)]].set(jnp.asarray(tallies, jnp.int32))

    tallies = jnp.where(number % 4 == 0, named(heavy_load, number // 4), named(usual, number - number // 4 - 1))
    mixed = jax.random.permutation(jax.random.fold_in(own, 3), amount)
    source_of, sink = mixed[0:amount // 2 * 2:2], mixed[1:amount // 2 * 2:2]
    room = jnp.minimum(tallies[source_of] - 1, most - tallies[sink]) // 2
    room = jnp.where((source_of == order[0]) | (sink == order[0]) | (tallies[sink] == 0), 0, jnp.maximum(room, 0))
    shifted = jax.random.randint(jax.random.fold_in(own, 4), (amount // 2,), 0, 1 << 20) % (room + 1)
    tallies = tallies.at[source_of].add(-shifted).at[sink].add(shifted)
    items = jnp.searchsorted(jnp.cumsum(tallies), jnp.arange(rows * top), side="right").astype(jnp.int32)
    listing = items.reshape(top, rows).T
    listing = listing[jax.random.permutation(jax.random.fold_in(own, 1), rows)]
    turn = jax.random.randint(jax.random.fold_in(own, 2), (rows, 1), 0, top)
    return jnp.take_along_axis(listing, (jnp.arange(top)[None, :] + turn) % top, axis=1)


def portions_of(amount, total, most, lean, full):
    weights = [(1 << 20) // math.isqrt(grade ** lean) + 1 for grade in range(1, amount + 1)]
    largest = most if full else min(most, max(-(-total // amount), total * weights[0] // sum(weights)))
    least = 1 if total - largest >= amount - 1 else 0
    counts, spare = [largest] + [least] * (amount - 1), total - largest - least * (amount - 1)
    while spare > 0:
        candidates = [i for i in range(1, amount) if counts[i] < largest] or [i for i in range(1, amount) if counts[i] < most]
        whole, remaining = sum([weights[i] for i in candidates]), spare
        for i in candidates:
            addition = min(most - counts[i], max(1, remaining * weights[i] // whole), spare)
            counts[i] = counts[i] + addition
            spare = spare - addition
    return np.array(counts)


def centred(own_key, extent, scale, reach, split=(), kind=jnp.bfloat16):
    gain = level_of(own_key, extent, split, -0.22, 0.18) if split else 1.0
    result = jax.random.normal(own_key, extent, jnp.float32) * scale * gain
    return jnp.minimum(jnp.maximum(result, -reach), reach).astype(kind)


def setup_inputs(seed: int = 0) -> dict:
    arg_keys = jax.random.split(jax.random.key(seed), 6)
    hidden = centred(arg_keys[0], (TOKENS, TOP, FF), 1.0, 6.0, ((0, 256),))
    routes_keys = jax.random.split(jax.random.fold_in(arg_keys[1], 1), TOKENS // TOK_DEV)
    routes_turns = jax.random.permutation(jax.random.fold_in(arg_keys[1], 3), TOKENS // TOK_DEV)
    routes = jax.vmap(lambda own, number: routed_block(jax.random.fold_in(arg_keys[1], 2), own, number, TOK_DEV, EXPERTS, TOP, MOST, 2))(routes_keys, routes_turns).reshape((TOKENS, TOP))
    gates = jnp.clip(jnp.exp(math.log(1.0) - 2.3025851 * jax.random.uniform(arg_keys[2], (TOKENS, TOP), jnp.float32) ** level_of(arg_keys[2], (TOKENS, TOP), ((0, 256),), -0.2, 0.2)), 0.1, 1.0)
    cotangent = centred(arg_keys[3], (TOKENS, D), 0.3, 1.796875, ((0, 256),))
    weight = centred(arg_keys[4], (EXPERTS, FF, D), D ** -0.5, 0.0625, ((0, 64), (2, 4)))
    return dict(hidden=hidden, routes=routes, gates=gates, cotangent=cotangent, weight=weight)


def reference(hidden, routes, gates, cotangent, weight):
    slot_count = TOKENS * TOP
    flat_experts = routes.reshape(slot_count).astype(jnp.int32)
    order_slots = jnp.argsort(flat_experts, stable=True).astype(jnp.int32)
    labels = jnp.arange(EXPERTS, dtype=jnp.int32)
    totals = jnp.sum((flat_experts[:, None] == labels[None, :]).astype(jnp.int32), axis=0).astype(jnp.int32)
    starts = (jnp.cumsum(totals) - totals).astype(jnp.int32)
    limit = N_DP * N_EXPERT * MOST
    padded_order = jnp.concatenate([order_slots, jnp.full((limit,), slot_count, jnp.int32)])
    scaled = (gates[:, :, None] * hidden.astype(jnp.float32)).astype(jnp.bfloat16).reshape(slot_count, FF)
    scaled_pad = jnp.concatenate([scaled, jnp.zeros((1, FF), jnp.bfloat16)], axis=0)
    cot_pad = jnp.concatenate([cotangent, jnp.zeros((1, D), jnp.bfloat16)], axis=0)

    def per_expert(expert_id):
        picked = lax.dynamic_slice_in_dim(padded_order, starts[expert_id], limit)
        valid = jnp.arange(limit, dtype=jnp.int32) < totals[expert_id]
        picked = jnp.where(valid, picked, slot_count).astype(jnp.int32)
        rows_cot = cot_pad[picked // TOP].astype(jnp.float32)
        matrix = weight[expert_id].astype(jnp.float32)
        back_rows = jnp.dot(rows_cot, matrix.T, precision=lax.Precision.HIGHEST)
        rows_scaled = scaled_pad[picked].astype(jnp.float32)
        grad_matrix = jnp.dot(rows_scaled.T, rows_cot, precision=lax.Precision.HIGHEST)
        return back_rows, grad_matrix.astype(jnp.bfloat16), picked

    back_rows, grad_weight, picked = lax.map(per_expert, labels)
    back_all = jnp.zeros((slot_count + 1, FF), jnp.float32).at[picked.reshape(-1)].set(back_rows.reshape(-1, FF))
    back = back_all[:slot_count]
    grad_hidden = (gates.reshape(slot_count)[:, None] * back).astype(jnp.bfloat16).reshape(TOKENS, TOP, FF)
    grad_gates = jnp.sum(hidden.reshape(slot_count, FF).astype(jnp.float32) * back, axis=1).reshape(TOKENS, TOP)
    return grad_hidden, grad_gates, grad_weight
```

```python
import jax
import jax.numpy as jnp
from jax import lax
from jax.sharding import PartitionSpec as P


def slots_for(flat_experts, columns, capacity):
    slot_count = flat_experts.shape[0]
    one_hot = (flat_experts[:, None] == jnp.arange(columns, dtype=jnp.int32)[None, :]).astype(
        jnp.int32
    )
    earlier = jnp.cumsum(one_hot, axis=0) - one_hot
    position = jnp.sum(earlier * one_hot, axis=1)
    destination = flat_experts * capacity + position
    slot_of = (
        jnp.full((columns * capacity,), slot_count, jnp.int32)
        .at[destination]
        .set(jnp.arange(slot_count, dtype=jnp.int32))
    )
    return destination, slot_of


def per_device(hidden, routes, gates, cotangent, weight):
    local_tokens, top_count, hidden_width = hidden.shape
    columns = lax.axis_size("expert")
    groups = lax.axis_size("dp")
    capacity = min(local_tokens, 2 * local_tokens * top_count // columns)
    slot_count = local_tokens * top_count
    quarter = cotangent.shape[1] // groups

    routes_all = lax.all_gather(routes.reshape(slot_count), "dp", axis=0, tiled=False)
    _, slot_of_all = jax.vmap(lambda r: slots_for(r, columns, capacity))(routes_all)
    destination, slot_of = slots_for(routes.reshape(slot_count), columns, capacity)

    cot_split = cotangent.reshape(local_tokens, groups, quarter).transpose(1, 0, 2)
    cot_q = lax.all_to_all(cot_split, "dp", split_axis=0, concat_axis=0, tiled=True)
    token_of = jnp.minimum(slot_of_all // top_count, local_tokens - 1)
    token_of = token_of.reshape(groups, columns, capacity).transpose(1, 0, 2)
    flat_token = token_of + (jnp.arange(groups, dtype=jnp.int32) * local_tokens)[None, :, None]
    send_cot = cot_q.reshape(groups * local_tokens, quarter)[flat_token]
    got_cot = lax.all_to_all(send_cot, "expert", split_axis=0, concat_axis=0, tiled=True)

    clamped = jnp.minimum(slot_of, slot_count - 1)
    send_hidden = hidden.reshape(slot_count, hidden_width)[clamped].reshape(
        columns, capacity, hidden_width
    )
    send_gates = jnp.where(slot_of < slot_count, gates.reshape(slot_count)[clamped], 0.0).reshape(
        columns, capacity
    )
    got_hidden = lax.all_to_all(send_hidden, "expert", split_axis=0, concat_axis=0, tiled=True)
    got_gates = lax.all_to_all(send_gates, "expert", split_axis=0, concat_axis=0, tiled=True)

    scaled = (got_gates[:, :, None] * got_hidden.astype(jnp.float32)).astype(jnp.bfloat16)
    rows_all = lax.all_gather(scaled, "dp", axis=0, tiled=False)
    matrix = weight[0]
    partial_back = jnp.stack(
        [
            jnp.einsum("scd,fd->scf", got_cot[:, g], matrix, preferred_element_type=jnp.float32)
            for g in range(groups)
        ]
    )
    back = lax.psum_scatter(partial_back, "dp", scatter_dimension=0, tiled=True)[0]
    grad_matrix = jnp.einsum(
        "gscf,sgcd->fd", rows_all, got_cot, preferred_element_type=jnp.float32
    )
    grad_hidden_rows = (got_gates[:, :, None] * back).astype(jnp.bfloat16)
    grad_gates_rows = jnp.sum(got_hidden.astype(jnp.float32) * back, axis=2)
    returned_hidden = lax.all_to_all(
        grad_hidden_rows, "expert", split_axis=0, concat_axis=0, tiled=True
    )
    returned_gates = lax.all_to_all(
        grad_gates_rows, "expert", split_axis=0, concat_axis=0, tiled=True
    )
    grad_hidden = returned_hidden.reshape(columns * capacity, hidden_width)[destination].reshape(
        local_tokens, top_count, hidden_width
    )
    grad_gates = returned_gates.reshape(columns * capacity)[destination].reshape(
        local_tokens, top_count
    )
    return (grad_hidden, grad_gates, grad_matrix.astype(jnp.bfloat16)[None])


def solution(mesh):
    placed = (
        P(("dp", "expert"), None, None),
        P(("dp", "expert"), None),
        P(("dp", "expert"), None),
        P(("dp", "expert"), None),
        P("expert", None, "dp"),
    )
    return jax.shard_map(
        per_device,
        mesh=mesh,
        in_specs=placed,
        out_specs=(
            P(("dp", "expert"), None, None),
            P(("dp", "expert"), None),
            P("expert", None, "dp"),
        ),
        check_vma=False,
    )
```

```python
import jax
import jax.numpy as jnp
from jax import lax
from jax.sharding import PartitionSpec as P


def slots_for(flat_experts, columns, capacity):
    slot_count = flat_experts.shape[0]
    one_hot = (flat_experts[:, None] == jnp.arange(columns, dtype=jnp.int32)[None, :]).astype(
        jnp.int32
    )
    earlier = jnp.cumsum(one_hot, axis=0) - one_hot
    position = jnp.sum(earlier * one_hot, axis=1)
    destination = flat_experts * capacity + position
    slot_of = (
        jnp.full((columns * capacity,), slot_count, jnp.int32)
        .at[destination]
        .set(jnp.arange(slot_count, dtype=jnp.int32))
    )
    return destination, slot_of


LANES = 128


def split3(values):
    pieces = []
    rest = values
    for _ in range(3):
        head = lax.reduce_precision(rest, exponent_bits=8, mantissa_bits=7)
        pieces.append(head.astype(jnp.bfloat16))
        rest = rest - head
    pad = jnp.zeros(values.shape + (LANES - 3,), jnp.bfloat16)
    return jnp.concatenate([jnp.stack(pieces, axis=-1), pad], axis=-1)


def join3(lanes):
    pieces = lanes[..., :3].astype(jnp.float32)
    return (pieces[..., 0] + pieces[..., 1]) + pieces[..., 2]


def per_device(hidden, routes, gates, cotangent, weight):
    local_tokens, top_count, hidden_width = hidden.shape
    columns = lax.axis_size("expert")
    groups = lax.axis_size("dp")
    capacity = min(local_tokens, 2 * local_tokens * top_count // columns)
    slot_count = local_tokens * top_count
    quarter = cotangent.shape[1] // groups

    destination, slot_of = slots_for(routes.reshape(slot_count), columns, capacity)

    route_lanes = jnp.zeros((local_tokens, LANES), jnp.bfloat16).at[:, :top_count].set(
        routes.astype(jnp.bfloat16)
    )
    cot_split = jnp.concatenate(
        [
            cotangent.reshape(local_tokens, groups, quarter).transpose(1, 0, 2),
            jnp.broadcast_to(route_lanes[None], (groups, local_tokens, LANES)),
        ],
        axis=2,
    )
    received = lax.all_to_all(cot_split, "dp", split_axis=0, concat_axis=0, tiled=True)
    cot_q = received[:, :, :quarter]
    routes_all = received[:, :, quarter : quarter + top_count].astype(jnp.int32)
    _, slot_of_all = jax.vmap(lambda r: slots_for(r, columns, capacity))(
        routes_all.reshape(groups, slot_count)
    )
    token_of = jnp.minimum(slot_of_all // top_count, local_tokens - 1)
    token_of = token_of.reshape(groups, columns, capacity).transpose(1, 0, 2)
    flat_token = token_of + (jnp.arange(groups, dtype=jnp.int32) * local_tokens)[None, :, None]
    send_cot = cot_q.reshape(groups * local_tokens, quarter)[flat_token]
    got_cot = lax.all_to_all(send_cot, "expert", split_axis=0, concat_axis=0, tiled=True)

    clamped = jnp.minimum(slot_of, slot_count - 1)
    send_hidden = hidden.reshape(slot_count, hidden_width)[clamped].reshape(
        columns, capacity, hidden_width
    )
    send_gates = jnp.where(slot_of < slot_count, gates.reshape(slot_count)[clamped], 0.0).reshape(
        columns, capacity
    )
    got = lax.all_to_all(
        jnp.concatenate([send_hidden, split3(send_gates)], axis=2),
        "expert",
        split_axis=0,
        concat_axis=0,
        tiled=True,
    )
    got_hidden = got[:, :, :hidden_width]
    got_gates = join3(got[:, :, hidden_width:])

    scaled = (got_gates[:, :, None] * got_hidden.astype(jnp.float32)).astype(jnp.bfloat16)
    rows_all = lax.all_gather(scaled, "dp", axis=0, tiled=False)
    matrix = weight[0]
    partial_back = jnp.stack(
        [
            jnp.einsum("scd,fd->scf", got_cot[:, g], matrix, preferred_element_type=jnp.float32)
            for g in range(groups)
        ]
    )
    back = lax.psum_scatter(partial_back, "dp", scatter_dimension=0, tiled=True)[0]
    grad_matrix = jnp.einsum(
        "gscf,sgcd->fd", rows_all, got_cot, preferred_element_type=jnp.float32
    )
    grad_hidden_rows = (got_gates[:, :, None] * back).astype(jnp.bfloat16)
    grad_gates_rows = jnp.sum(got_hidden.astype(jnp.float32) * back, axis=2)
    returned = lax.all_to_all(
        jnp.concatenate([grad_hidden_rows, split3(grad_gates_rows)], axis=2),
        "expert",
        split_axis=0,
        concat_axis=0,
        tiled=True,
    )
    returned_hidden = returned[:, :, :hidden_width]
    returned_gates = join3(returned[:, :, hidden_width:])
    grad_hidden = returned_hidden.reshape(columns * capacity, hidden_width)[destination].reshape(
        local_tokens, top_count, hidden_width
    )
    grad_gates = returned_gates.reshape(columns * capacity)[destination].reshape(
        local_tokens, top_count
    )
    return (grad_hidden, grad_gates, grad_matrix.astype(jnp.bfloat16)[None])


def solution(mesh):
    placed = (
        P(("dp", "expert"), None, None),
        P(("dp", "expert"), None),
        P(("dp", "expert"), None),
        P(("dp", "expert"), None),
        P("expert", None, "dp"),
    )
    return jax.shard_map(
        per_device,
        mesh=mesh,
        in_specs=placed,
        out_specs=(
            P(("dp", "expert"), None, None),
            P(("dp", "expert"), None),
            P("expert", None, "dp"),
        ),
        check_vma=False,
    )
```

```python
import jax
import jax.numpy as jnp
from jax import lax
from jax.sharding import PartitionSpec as P


def slots_for(flat_experts, columns, capacity):
    slot_count = flat_experts.shape[0]
    one_hot = (flat_experts[:, None] == jnp.arange(columns, dtype=jnp.int32)[None, :]).astype(
        jnp.int32
    )
    earlier = jnp.cumsum(one_hot, axis=0) - one_hot
    position = jnp.sum(earlier * one_hot, axis=1)
    destination = flat_experts * capacity + position
    slot_of = (
        jnp.full((columns * capacity,), slot_count, jnp.int32)
        .at[destination]
        .set(jnp.arange(slot_count, dtype=jnp.int32))
    )
    return destination, slot_of


LANES = 128
CHUNKS = 2


def split3(values):
    pieces = []
    rest = values
    for _ in range(3):
        head = lax.reduce_precision(rest, exponent_bits=8, mantissa_bits=7)
        pieces.append(head.astype(jnp.bfloat16))
        rest = rest - head
    pad = jnp.zeros(values.shape + (LANES - 3,), jnp.bfloat16)
    return jnp.concatenate([jnp.stack(pieces, axis=-1), pad], axis=-1)


def join3(lanes):
    pieces = lanes[..., :3].astype(jnp.float32)
    return (pieces[..., 0] + pieces[..., 1]) + pieces[..., 2]


def per_device(hidden, routes, gates, cotangent, weight):
    local_tokens, top_count, hidden_width = hidden.shape
    columns = lax.axis_size("expert")
    groups = lax.axis_size("dp")
    capacity = min(local_tokens, 2 * local_tokens * top_count // columns)
    slot_count = local_tokens * top_count
    quarter = cotangent.shape[1] // groups

    destination, slot_of = slots_for(routes.reshape(slot_count), columns, capacity)

    route_lanes = jnp.zeros((local_tokens, LANES), jnp.bfloat16).at[:, :top_count].set(
        routes.astype(jnp.bfloat16)
    )
    cot_split = jnp.concatenate(
        [
            cotangent.reshape(local_tokens, groups, quarter).transpose(1, 0, 2),
            jnp.broadcast_to(route_lanes[None], (groups, local_tokens, LANES)),
        ],
        axis=2,
    )
    received = lax.all_to_all(cot_split, "dp", split_axis=0, concat_axis=0, tiled=True)
    clamped = jnp.minimum(slot_of, slot_count - 1)
    send_hidden = hidden.reshape(slot_count, hidden_width)[clamped].reshape(
        columns, capacity, hidden_width
    )
    send_gates = jnp.where(slot_of < slot_count, gates.reshape(slot_count)[clamped], 0.0).reshape(
        columns, capacity
    )
    got = lax.all_to_all(
        jnp.concatenate([send_hidden, split3(send_gates)], axis=2),
        "expert",
        split_axis=0,
        concat_axis=0,
        tiled=True,
    )
    got, received = lax.optimization_barrier((got, received))
    got_hidden = got[:, :, :hidden_width]
    got_gates = join3(got[:, :, hidden_width:])
    scaled = (got_gates[:, :, None] * got_hidden.astype(jnp.float32)).astype(jnp.bfloat16)
    rows_all = lax.all_gather(scaled, "dp", axis=0, tiled=False)

    cot_q = received[:, :, :quarter]
    routes_all = received[:, :, quarter : quarter + top_count].astype(jnp.int32)
    _, slot_of_all = jax.vmap(lambda r: slots_for(r, columns, capacity))(
        routes_all.reshape(groups, slot_count)
    )
    token_of = jnp.minimum(slot_of_all // top_count, local_tokens - 1)
    token_of = token_of.reshape(groups, columns, capacity).transpose(1, 0, 2)
    flat_token = token_of + (jnp.arange(groups, dtype=jnp.int32) * local_tokens)[None, :, None]
    send_cot = cot_q.reshape(groups * local_tokens, quarter)[flat_token]

    matrix = weight[0]
    step = capacity // CHUNKS
    backs, got_chunks = [], []
    for c in range(CHUNKS):
        got_cot = lax.all_to_all(
            send_cot[:, :, c * step : (c + 1) * step],
            "expert",
            split_axis=0,
            concat_axis=0,
            tiled=True,
        )
        if c == 0:
            rows_all, got_cot = lax.optimization_barrier((rows_all, got_cot))
        got_chunks.append(got_cot)
        partial_back = jnp.stack(
            [
                jnp.einsum(
                    "scd,fd->scf", got_cot[:, g], matrix, preferred_element_type=jnp.float32
                )
                for g in range(groups)
            ]
        )
        backs.append(lax.psum_scatter(partial_back, "dp", scatter_dimension=0, tiled=True)[0])
    grad_matrix = sum(
        jnp.einsum(
            "gscf,sgcd->fd",
            rows_all[:, :, c * step : (c + 1) * step],
            got_chunks[c],
            preferred_element_type=jnp.float32,
        )
        for c in range(CHUNKS)
    )
    back = jnp.concatenate(backs, axis=1)
    grad_hidden_rows = (got_gates[:, :, None] * back).astype(jnp.bfloat16)
    grad_gates_rows = jnp.sum(got_hidden.astype(jnp.float32) * back, axis=2)
    returned = lax.all_to_all(
        jnp.concatenate([grad_hidden_rows, split3(grad_gates_rows)], axis=2),
        "expert",
        split_axis=0,
        concat_axis=0,
        tiled=True,
    )
    returned_hidden = returned[:, :, :hidden_width]
    returned_gates = join3(returned[:, :, hidden_width:])
    grad_hidden = returned_hidden.reshape(columns * capacity, hidden_width)[destination].reshape(
        local_tokens, top_count, hidden_width
    )
    grad_gates = returned_gates.reshape(columns * capacity)[destination].reshape(
        local_tokens, top_count
    )
    return (grad_hidden, grad_gates, grad_matrix.astype(jnp.bfloat16)[None])


def solution(mesh):
    placed = (
        P(("dp", "expert"), None, None),
        P(("dp", "expert"), None),
        P(("dp", "expert"), None),
        P(("dp", "expert"), None),
        P("expert", None, "dp"),
    )
    return jax.shard_map(
        per_device,
        mesh=mesh,
        in_specs=placed,
        out_specs=(
            P(("dp", "expert"), None, None),
            P(("dp", "expert"), None),
            P("expert", None, "dp"),
        ),
        check_vma=False,
    )
```

```python
import jax
import jax.numpy as jnp
from jax import lax
from jax.sharding import PartitionSpec as P


def slots_for(flat_experts, columns, capacity):
    slot_count = flat_experts.shape[0]
    one_hot = (flat_experts[:, None] == jnp.arange(columns, dtype=jnp.int32)[None, :]).astype(
        jnp.int32
    )
    earlier = jnp.cumsum(one_hot, axis=0) - one_hot
    position = jnp.sum(earlier * one_hot, axis=1)
    destination = flat_experts * capacity + position
    slot_of = (
        jnp.full((columns * capacity,), slot_count, jnp.int32)
        .at[destination]
        .set(jnp.arange(slot_count, dtype=jnp.int32))
    )
    return destination, slot_of


LANES = 128
CHUNKS = 2


def split3(values):
    pieces = []
    rest = values
    for _ in range(3):
        head = lax.reduce_precision(rest, exponent_bits=8, mantissa_bits=7)
        pieces.append(head.astype(jnp.bfloat16))
        rest = rest - head
    pad = jnp.zeros(values.shape + (LANES - 3,), jnp.bfloat16)
    return jnp.concatenate([jnp.stack(pieces, axis=-1), pad], axis=-1)


def join3(lanes):
    pieces = lanes[..., :3].astype(jnp.float32)
    return (pieces[..., 0] + pieces[..., 1]) + pieces[..., 2]


def per_device(hidden, routes, gates, cotangent, weight):
    local_tokens, top_count, hidden_width = hidden.shape
    columns = lax.axis_size("expert")
    groups = lax.axis_size("dp")
    capacity = min(local_tokens, 2 * local_tokens * top_count // columns)
    slot_count = local_tokens * top_count
    quarter = cotangent.shape[1] // groups

    destination, slot_of = slots_for(routes.reshape(slot_count), columns, capacity)

    route_lanes = jnp.zeros((local_tokens, LANES), jnp.bfloat16).at[:, :top_count].set(
        routes.astype(jnp.bfloat16)
    )
    cot_split = jnp.concatenate(
        [
            cotangent.reshape(local_tokens, groups, quarter).transpose(1, 0, 2),
            jnp.broadcast_to(route_lanes[None], (groups, local_tokens, LANES)),
        ],
        axis=2,
    )
    received = lax.all_to_all(cot_split, "dp", split_axis=0, concat_axis=0, tiled=True)
    routes_all = received[:, :, quarter : quarter + top_count].astype(jnp.int32)
    _, slot_of_all = jax.vmap(lambda r: slots_for(r, columns, capacity))(
        routes_all.reshape(groups, slot_count)
    )

    gate_lanes = split3(gates.reshape(slot_count))
    hidden_rows = jnp.concatenate(
        [
            hidden.reshape(slot_count, hidden_width),
            gate_lanes,
            jnp.zeros((slot_count, quarter - hidden_width - LANES), jnp.bfloat16),
        ],
        axis=1,
    )
    cot_rows = groups * local_tokens
    zero_row = cot_rows + slot_count
    table = jnp.concatenate(
        [
            received[:, :, :quarter].reshape(cot_rows, quarter),
            hidden_rows,
            jnp.zeros((8, quarter), jnp.bfloat16),
        ],
        axis=0,
    )
    token_of = slot_of_all // top_count + (jnp.arange(groups, dtype=jnp.int32) * local_tokens)[
        :, None
    ]
    token_of = jnp.where(slot_of_all < slot_count, token_of, zero_row)
    token_of = token_of.reshape(groups, columns, capacity).transpose(1, 0, 2)
    hidden_of = jnp.where(slot_of < slot_count, slot_of + cot_rows, zero_row).reshape(
        columns, capacity
    )

    matrix = weight[0]
    bounds = [0, capacity // 2, capacity]
    backs, got_chunks = [], []
    for c in range(len(bounds) - 1):
        step = bounds[c + 1] - bounds[c]
        index = token_of[:, :, bounds[c] : bounds[c + 1]].reshape(columns, groups * step)
        if c == 0:
            index = jnp.concatenate([index, hidden_of], axis=1)
        got_rows = lax.all_to_all(table[index], "expert", split_axis=0, concat_axis=0, tiled=True)
        if c == 0:
            got_hidden = got_rows[:, groups * step :, :hidden_width]
            got_gates = join3(got_rows[:, groups * step :, hidden_width : hidden_width + LANES])
            scaled = (got_gates[:, :, None] * got_hidden.astype(jnp.float32)).astype(
                jnp.bfloat16
            )
            rows_all = lax.all_gather(scaled, "dp", axis=0, tiled=False)
        if c == 1:
            rows_all, got_rows = lax.optimization_barrier((rows_all, got_rows))
        got_cot = got_rows[:, : groups * step].reshape(columns, groups, step, quarter)
        got_chunks.append(got_cot)
        partial_back = jnp.stack(
            [
                jnp.einsum(
                    "scd,fd->scf", got_cot[:, g], matrix, preferred_element_type=jnp.float32
                )
                for g in range(groups)
            ]
        )
        backs.append(lax.psum_scatter(partial_back, "dp", scatter_dimension=0, tiled=True)[0])
    grad_matrix = sum(
        jnp.einsum(
            "gscf,sgcd->fd",
            rows_all[:, :, bounds[c] : bounds[c + 1]],
            got_chunks[c],
            preferred_element_type=jnp.float32,
        )
        for c in range(len(bounds) - 1)
    )
    back = jnp.concatenate(backs, axis=1)
    grad_matrix, back = lax.optimization_barrier((grad_matrix, back))
    grad_hidden_rows = (got_gates[:, :, None] * back).astype(jnp.bfloat16)
    grad_gates_rows = jnp.sum(got_hidden.astype(jnp.float32) * back, axis=2)
    returned = lax.all_to_all(
        jnp.concatenate([grad_hidden_rows, split3(grad_gates_rows)], axis=2),
        "expert",
        split_axis=0,
        concat_axis=0,
        tiled=True,
    )
    returned_hidden = returned[:, :, :hidden_width]
    returned_gates = join3(returned[:, :, hidden_width:])
    grad_hidden = returned_hidden.reshape(columns * capacity, hidden_width)[destination].reshape(
        local_tokens, top_count, hidden_width
    )
    grad_gates = returned_gates.reshape(columns * capacity)[destination].reshape(
        local_tokens, top_count
    )
    return (grad_hidden, grad_gates, grad_matrix.astype(jnp.bfloat16)[None])


def solution(mesh):
    placed = (
        P(("dp", "expert"), None, None),
        P(("dp", "expert"), None),
        P(("dp", "expert"), None),
        P(("dp", "expert"), None),
        P("expert", None, "dp"),
    )
    return jax.shard_map(
        per_device,
        mesh=mesh,
        in_specs=placed,
        out_specs=(
            P(("dp", "expert"), None, None),
            P(("dp", "expert"), None),
            P("expert", None, "dp"),
        ),
        check_vma=False,
    )
```

```python
import jax
import jax.numpy as jnp
from jax import lax
from jax.sharding import PartitionSpec as P


def slots_for(flat_experts, columns, capacity):
    slot_count = flat_experts.shape[0]
    one_hot = (flat_experts[:, None] == jnp.arange(columns, dtype=jnp.int32)[None, :]).astype(
        jnp.int32
    )
    earlier = jnp.cumsum(one_hot, axis=0) - one_hot
    position = jnp.sum(earlier * one_hot, axis=1)
    destination = flat_experts * capacity + position
    slot_of = (
        jnp.full((columns * capacity,), slot_count, jnp.int32)
        .at[destination]
        .set(jnp.arange(slot_count, dtype=jnp.int32))
    )
    return destination, slot_of


LANES = 128
CHUNKS = 2


def split3(values, lanes=LANES):
    pieces = []
    rest = values
    for _ in range(3):
        head = lax.reduce_precision(rest, exponent_bits=8, mantissa_bits=7)
        pieces.append(head.astype(jnp.bfloat16))
        rest = rest - head
    terms = jnp.stack(pieces, axis=-1)
    if lanes == 3:
        return terms
    pad = jnp.zeros(values.shape + (lanes - 3,), jnp.bfloat16)
    return jnp.concatenate([terms, pad], axis=-1)


def join3(lanes):
    pieces = lanes[..., :3].astype(jnp.float32)
    return (pieces[..., 0] + pieces[..., 1]) + pieces[..., 2]


def per_device(hidden, routes, gates, cotangent, weight):
    local_tokens, top_count, hidden_width = hidden.shape
    columns = lax.axis_size("expert")
    groups = lax.axis_size("dp")
    capacity = min(local_tokens, 2 * local_tokens * top_count // columns)
    slot_count = local_tokens * top_count
    quarter = cotangent.shape[1] // groups

    destination, slot_of = slots_for(routes.reshape(slot_count), columns, capacity)

    route_lanes = jnp.zeros((local_tokens, LANES), jnp.bfloat16).at[:, :top_count].set(
        routes.astype(jnp.bfloat16)
    )
    cot_split = jnp.concatenate(
        [
            cotangent.reshape(local_tokens, groups, quarter).transpose(1, 0, 2),
            jnp.broadcast_to(route_lanes[None], (groups, local_tokens, LANES)),
        ],
        axis=2,
    )
    received = lax.all_to_all(cot_split, "dp", split_axis=0, concat_axis=0, tiled=True)
    routes_all = received[:, :, quarter : quarter + top_count].astype(jnp.int32)
    _, slot_of_all = jax.vmap(lambda r: slots_for(r, columns, capacity))(
        routes_all.reshape(groups, slot_count)
    )

    cot_rows = groups * local_tokens
    table = jnp.concatenate(
        [received[:, :, :quarter].reshape(cot_rows, quarter), jnp.zeros((8, quarter), jnp.bfloat16)],
        axis=0,
    )
    token_of = slot_of_all // top_count + (jnp.arange(groups, dtype=jnp.int32) * local_tokens)[
        :, None
    ]
    token_of = jnp.where(slot_of_all < slot_count, token_of, cot_rows)
    token_of = token_of.reshape(groups, columns, capacity).transpose(1, 0, 2)

    clamped = jnp.minimum(slot_of, slot_count - 1)
    send_hidden = hidden.reshape(slot_count, hidden_width)[clamped].reshape(
        columns, capacity * hidden_width
    )
    send_gates = jnp.where(slot_of < slot_count, gates.reshape(slot_count)[clamped], 0.0)
    gate_terms = split3(send_gates, 3).reshape(columns, capacity * 3)
    packed = capacity * hidden_width + capacity * 3
    packed_rows = -(-packed // quarter)
    hidden_rows = jnp.concatenate(
        [
            send_hidden,
            gate_terms,
            jnp.zeros((columns, packed_rows * quarter - packed), jnp.bfloat16),
        ],
        axis=1,
    ).reshape(columns, packed_rows, quarter)

    matrix = weight[0]
    bounds = [0, capacity // 2, capacity]
    backs, got_chunks = [], []
    for c in range(len(bounds) - 1):
        step = bounds[c + 1] - bounds[c]
        index = token_of[:, :, bounds[c] : bounds[c + 1]].reshape(columns, groups * step)
        payload = table[index]
        if c == 0:
            payload = jnp.concatenate([payload, hidden_rows], axis=1)
        got_rows = lax.all_to_all(payload, "expert", split_axis=0, concat_axis=0, tiled=True)
        if c == 0:
            got_packed = got_rows[:, groups * step :].reshape(columns, packed_rows * quarter)
            got_hidden = got_packed[:, : capacity * hidden_width].reshape(
                columns, capacity, hidden_width
            )
            got_gates = join3(
                got_packed[:, capacity * hidden_width : packed].reshape(columns, capacity, 3)
            )
            scaled = (got_gates[:, :, None] * got_hidden.astype(jnp.float32)).astype(
                jnp.bfloat16
            )
            rows_all = lax.all_gather(scaled, "dp", axis=0, tiled=False)
        if c == 1:
            rows_all, got_rows = lax.optimization_barrier((rows_all, got_rows))
        got_cot = got_rows[:, : groups * step].reshape(columns, groups, step, quarter)
        got_chunks.append(got_cot)
        partial_back = jnp.stack(
            [
                jnp.einsum(
                    "scd,fd->scf", got_cot[:, g], matrix, preferred_element_type=jnp.float32
                )
                for g in range(groups)
            ]
        )
        backs.append(lax.psum_scatter(partial_back, "dp", scatter_dimension=0, tiled=True)[0])
    grad_matrix = sum(
        jnp.einsum(
            "gscf,sgcd->fd",
            rows_all[:, :, bounds[c] : bounds[c + 1]],
            got_chunks[c],
            preferred_element_type=jnp.float32,
        )
        for c in range(len(bounds) - 1)
    )
    back = jnp.concatenate(backs, axis=1)
    grad_matrix, back = lax.optimization_barrier((grad_matrix, back))
    grad_hidden_rows = (got_gates[:, :, None] * back).astype(jnp.bfloat16)
    grad_gates_rows = jnp.sum(got_hidden.astype(jnp.float32) * back, axis=2)
    returned = lax.all_to_all(
        jnp.concatenate([grad_hidden_rows, split3(grad_gates_rows)], axis=2),
        "expert",
        split_axis=0,
        concat_axis=0,
        tiled=True,
    )
    returned_hidden = returned[:, :, :hidden_width]
    returned_gates = join3(returned[:, :, hidden_width:])
    grad_hidden = returned_hidden.reshape(columns * capacity, hidden_width)[destination].reshape(
        local_tokens, top_count, hidden_width
    )
    grad_gates = returned_gates.reshape(columns * capacity)[destination].reshape(
        local_tokens, top_count
    )
    return (grad_hidden, grad_gates, grad_matrix.astype(jnp.bfloat16)[None])


def solution(mesh):
    placed = (
        P(("dp", "expert"), None, None),
        P(("dp", "expert"), None),
        P(("dp", "expert"), None),
        P(("dp", "expert"), None),
        P("expert", None, "dp"),
    )
    return jax.shard_map(
        per_device,
        mesh=mesh,
        in_specs=placed,
        out_specs=(
            P(("dp", "expert"), None, None),
            P(("dp", "expert"), None),
            P("expert", None, "dp"),
        ),
        check_vma=False,
    )
```

```python
import jax
import jax.numpy as jnp
from jax import lax
from jax.sharding import PartitionSpec as P


def slots_for(flat_experts, columns, capacity):
    slot_count = flat_experts.shape[0]
    one_hot = (flat_experts[:, None] == jnp.arange(columns, dtype=jnp.int32)[None, :]).astype(
        jnp.int32
    )
    earlier = jnp.cumsum(one_hot, axis=0) - one_hot
    position = jnp.sum(earlier * one_hot, axis=1)
    destination = flat_experts * capacity + position
    slot_of = (
        jnp.full((columns * capacity,), slot_count, jnp.int32)
        .at[destination]
        .set(jnp.arange(slot_count, dtype=jnp.int32))
    )
    return destination, slot_of


def per_device(hidden, routes, gates, cotangent, weight):
    local_tokens, top_count, hidden_width = hidden.shape
    columns = lax.axis_size("expert")
    groups = lax.axis_size("dp")
    capacity = min(local_tokens, 2 * local_tokens * top_count // columns)
    slot_count = local_tokens * top_count
    quarter = cotangent.shape[1] // groups

    routes_all = lax.all_gather(routes.reshape(slot_count), "dp", axis=0, tiled=False)
    _, slot_of_all = jax.vmap(lambda r: slots_for(r, columns, capacity))(routes_all)
    destination, slot_of = slots_for(routes.reshape(slot_count), columns, capacity)

    cot_split = cotangent.reshape(local_tokens, groups, quarter).transpose(1, 0, 2)
    cot_q = lax.all_to_all(cot_split, "dp", split_axis=0, concat_axis=0, tiled=True)
    token_of = jnp.minimum(slot_of_all // top_count, local_tokens - 1)
    token_of = token_of.reshape(groups, columns, capacity).transpose(1, 0, 2)
    flat_token = token_of + (jnp.arange(groups, dtype=jnp.int32) * local_tokens)[None, :, None]
    send_cot = cot_q.reshape(groups * local_tokens, quarter)[flat_token]
    got_cot = lax.all_to_all(send_cot, "expert", split_axis=0, concat_axis=0, tiled=True)

    clamped = jnp.minimum(slot_of, slot_count - 1)
    send_hidden = hidden.reshape(slot_count, hidden_width)[clamped].reshape(
        columns, capacity, hidden_width
    )
    send_gates = jnp.where(slot_of < slot_count, gates.reshape(slot_count)[clamped], 0.0).reshape(
        columns, capacity
    )
    got_hidden = lax.all_to_all(send_hidden, "expert", split_axis=0, concat_axis=0, tiled=True)
    got_gates = lax.all_to_all(send_gates, "expert", split_axis=0, concat_axis=0, tiled=True)

    scaled = (got_gates[:, :, None] * got_hidden.astype(jnp.float32)).astype(jnp.bfloat16)
    rows_all = lax.all_gather(scaled, "dp", axis=0, tiled=False)
    matrix = weight[0]
    partial_back = jnp.stack(
        [
            jnp.einsum("scd,fd->scf", got_cot[:, g], matrix, preferred_element_type=jnp.float32)
            for g in range(groups)
        ]
    )
    parts = lax.all_to_all(
        partial_back.astype(jnp.bfloat16), "dp", split_axis=0, concat_axis=0, tiled=True
    )
    back = jnp.sum(parts.astype(jnp.float32), axis=0)
    grad_matrix = jnp.einsum(
        "gscf,sgcd->fd", rows_all, got_cot, preferred_element_type=jnp.float32
    )
    grad_hidden_rows = (got_gates[:, :, None] * back).astype(jnp.bfloat16)
    grad_gates_rows = jnp.sum(got_hidden.astype(jnp.float32) * back, axis=2)
    returned_hidden = lax.all_to_all(
        grad_hidden_rows, "expert", split_axis=0, concat_axis=0, tiled=True
    )
    returned_gates = lax.all_to_all(
        grad_gates_rows, "expert", split_axis=0, concat_axis=0, tiled=True
    )
    grad_hidden = returned_hidden.reshape(columns * capacity, hidden_width)[destination].reshape(
        local_tokens, top_count, hidden_width
    )
    grad_gates = returned_gates.reshape(columns * capacity)[destination].reshape(
        local_tokens, top_count
    )
    return (grad_hidden, grad_gates, grad_matrix.astype(jnp.bfloat16)[None])


def solution(mesh):
    placed = (
        P(("dp", "expert"), None, None),
        P(("dp", "expert"), None),
        P(("dp", "expert"), None),
        P(("dp", "expert"), None),
        P("expert", None, "dp"),
    )
    return jax.shard_map(
        per_device,
        mesh=mesh,
        in_specs=placed,
        out_specs=(
            P(("dp", "expert"), None, None),
            P(("dp", "expert"), None),
            P("expert", None, "dp"),
        ),
        check_vma=False,
    )
```

```python
import jax
import jax.numpy as jnp
from jax import lax
from jax.sharding import PartitionSpec as P


def slots_for(flat_experts, columns, capacity):
    slot_count = flat_experts.shape[0]
    one_hot = (flat_experts[:, None] == jnp.arange(columns, dtype=jnp.int32)[None, :]).astype(
        jnp.int32
    )
    earlier = jnp.cumsum(one_hot, axis=0) - one_hot
    position = jnp.sum(earlier * one_hot, axis=1)
    destination = flat_experts * capacity + position
    slot_of = (
        jnp.full((columns * capacity,), slot_count, jnp.int32)
        .at[destination]
        .set(jnp.arange(slot_count, dtype=jnp.int32))
    )
    return destination, slot_of


LANES = 128
CHUNKS = 2


def split3(values):
    pieces = []
    rest = values
    for _ in range(3):
        head = lax.reduce_precision(rest, exponent_bits=8, mantissa_bits=7)
        pieces.append(head.astype(jnp.bfloat16))
        rest = rest - head
    pad = jnp.zeros(values.shape + (LANES - 3,), jnp.bfloat16)
    return jnp.concatenate([jnp.stack(pieces, axis=-1), pad], axis=-1)


def join3(lanes):
    pieces = lanes[..., :3].astype(jnp.float32)
    return (pieces[..., 0] + pieces[..., 1]) + pieces[..., 2]


def per_device(hidden, routes, gates, cotangent, weight):
    local_tokens, top_count, hidden_width = hidden.shape
    columns = lax.axis_size("expert")
    groups = lax.axis_size("dp")
    capacity = min(local_tokens, 2 * local_tokens * top_count // columns)
    slot_count = local_tokens * top_count
    quarter = cotangent.shape[1] // groups

    destination, slot_of = slots_for(routes.reshape(slot_count), columns, capacity)

    route_lanes = jnp.zeros((local_tokens, LANES), jnp.bfloat16).at[:, :top_count].set(
        routes.astype(jnp.bfloat16)
    )
    cot_split = jnp.concatenate(
        [
            cotangent.reshape(local_tokens, groups, quarter).transpose(1, 0, 2),
            jnp.broadcast_to(route_lanes[None], (groups, local_tokens, LANES)),
        ],
        axis=2,
    )
    received = lax.all_to_all(cot_split, "dp", split_axis=0, concat_axis=0, tiled=True)
    routes_all = received[:, :, quarter : quarter + top_count].astype(jnp.int32)
    _, slot_of_all = jax.vmap(lambda r: slots_for(r, columns, capacity))(
        routes_all.reshape(groups, slot_count)
    )

    gate_lanes = split3(gates.reshape(slot_count))
    hidden_rows = jnp.concatenate(
        [
            hidden.reshape(slot_count, hidden_width),
            gate_lanes,
            jnp.zeros((slot_count, quarter - hidden_width - LANES), jnp.bfloat16),
        ],
        axis=1,
    )
    cot_rows = groups * local_tokens
    zero_row = cot_rows + slot_count
    table = jnp.concatenate(
        [
            received[:, :, :quarter].reshape(cot_rows, quarter),
            hidden_rows,
            jnp.zeros((8, quarter), jnp.bfloat16),
        ],
        axis=0,
    )
    token_of = slot_of_all // top_count + (jnp.arange(groups, dtype=jnp.int32) * local_tokens)[
        :, None
    ]
    token_of = jnp.where(slot_of_all < slot_count, token_of, zero_row)
    token_of = token_of.reshape(groups, columns, capacity).transpose(1, 0, 2)
    hidden_of = jnp.where(slot_of < slot_count, slot_of + cot_rows, zero_row).reshape(
        columns, capacity
    )

    matrix = weight[0]
    bounds = [0, capacity // 2, capacity * 3 // 4, capacity]
    backs, got_chunks = [], []
    for c in range(len(bounds) - 1):
        step = bounds[c + 1] - bounds[c]
        index = token_of[:, :, bounds[c] : bounds[c + 1]].reshape(columns, groups * step)
        if c == 0:
            index = jnp.concatenate([index, hidden_of], axis=1)
        payload = table[index]
        if c > 0:
            payload, pending = lax.optimization_barrier((payload, pending))
            backs.append(lax.psum_scatter(pending, "dp", scatter_dimension=0, tiled=True)[0])
        got_rows = lax.all_to_all(payload, "expert", split_axis=0, concat_axis=0, tiled=True)
        if c == 0:
            got_hidden = got_rows[:, groups * step :, :hidden_width]
            got_gates = join3(got_rows[:, groups * step :, hidden_width : hidden_width + LANES])
            scaled = (got_gates[:, :, None] * got_hidden.astype(jnp.float32)).astype(
                jnp.bfloat16
            )
            rows_all = lax.all_gather(scaled, "dp", axis=0, tiled=False)
        if c == 1:
            rows_all, got_rows = lax.optimization_barrier((rows_all, got_rows))
        got_cot = got_rows[:, : groups * step].reshape(columns, groups, step, quarter)
        got_chunks.append(got_cot)
        partial_back = jnp.stack(
            [
                jnp.einsum(
                    "scd,fd->scf", got_cot[:, g], matrix, preferred_element_type=jnp.float32
                )
                for g in range(groups)
            ]
        )
        pending = partial_back
    backs.append(lax.psum_scatter(pending, "dp", scatter_dimension=0, tiled=True)[0])
    grad_matrix = sum(
        jnp.einsum(
            "gscf,sgcd->fd",
            rows_all[:, :, bounds[c] : bounds[c + 1]],
            got_chunks[c],
            preferred_element_type=jnp.float32,
        )
        for c in range(len(bounds) - 1)
    )
    back = jnp.concatenate(backs, axis=1)
    grad_matrix, back = lax.optimization_barrier((grad_matrix, back))
    grad_hidden_rows = (got_gates[:, :, None] * back).astype(jnp.bfloat16)
    grad_gates_rows = jnp.sum(got_hidden.astype(jnp.float32) * back, axis=2)
    returned = lax.all_to_all(
        jnp.concatenate([grad_hidden_rows, split3(grad_gates_rows)], axis=2),
        "expert",
        split_axis=0,
        concat_axis=0,
        tiled=True,
    )
    returned_hidden = returned[:, :, :hidden_width]
    returned_gates = join3(returned[:, :, hidden_width:])
    grad_hidden = returned_hidden.reshape(columns * capacity, hidden_width)[destination].reshape(
        local_tokens, top_count, hidden_width
    )
    grad_gates = returned_gates.reshape(columns * capacity)[destination].reshape(
        local_tokens, top_count
    )
    return (grad_hidden, grad_gates, grad_matrix.astype(jnp.bfloat16)[None])


def solution(mesh):
    placed = (
        P(("dp", "expert"), None, None),
        P(("dp", "expert"), None),
        P(("dp", "expert"), None),
        P(("dp", "expert"), None),
        P("expert", None, "dp"),
    )
    return jax.shard_map(
        per_device,
        mesh=mesh,
        in_specs=placed,
        out_specs=(
            P(("dp", "expert"), None, None),
            P(("dp", "expert"), None),
            P("expert", None, "dp"),
        ),
        check_vma=False,
    )
```

```python
import jax
import jax.numpy as jnp
from jax import lax
from jax.sharding import PartitionSpec as P


def slots_for(flat_experts, columns, capacity):
    slot_count = flat_experts.shape[0]
    one_hot = (flat_experts[:, None] == jnp.arange(columns, dtype=jnp.int32)[None, :]).astype(
        jnp.int32
    )
    earlier = jnp.cumsum(one_hot, axis=0) - one_hot
    position = jnp.sum(earlier * one_hot, axis=1)
    destination = flat_experts * capacity + position
    slot_of = (
        jnp.full((columns * capacity,), slot_count, jnp.int32)
        .at[destination]
        .set(jnp.arange(slot_count, dtype=jnp.int32))
    )
    return destination, slot_of


LANES = 128


def split3(values):
    pieces = []
    rest = values
    for _ in range(3):
        head = lax.reduce_precision(rest, exponent_bits=8, mantissa_bits=7)
        pieces.append(head.astype(jnp.bfloat16))
        rest = rest - head
    pad = jnp.zeros(values.shape + (LANES - 3,), jnp.bfloat16)
    return jnp.concatenate([jnp.stack(pieces, axis=-1), pad], axis=-1)


def join3(lanes):
    pieces = lanes[..., :3].astype(jnp.float32)
    return (pieces[..., 0] + pieces[..., 1]) + pieces[..., 2]


def per_device(hidden, routes, gates, cotangent, weight):
    local_tokens, top_count, hidden_width = hidden.shape
    columns = lax.axis_size("expert")
    groups = lax.axis_size("dp")
    capacity = min(local_tokens, 2 * local_tokens * top_count // columns)
    slot_count = local_tokens * top_count
    quarter = cotangent.shape[1] // groups

    destination, slot_of = slots_for(routes.reshape(slot_count), columns, capacity)

    route_lanes = jnp.zeros((local_tokens, LANES), jnp.bfloat16).at[:, :top_count].set(
        routes.astype(jnp.bfloat16)
    )
    cot_split = jnp.concatenate(
        [
            cotangent.reshape(local_tokens, groups, quarter).transpose(1, 0, 2),
            jnp.broadcast_to(route_lanes[None], (groups, local_tokens, LANES)),
        ],
        axis=2,
    )
    received = lax.all_to_all(cot_split, "dp", split_axis=0, concat_axis=0, tiled=True)
    cot_q = received[:, :, :quarter]
    routes_all = received[:, :, quarter : quarter + top_count].astype(jnp.int32)
    _, slot_of_all = jax.vmap(lambda r: slots_for(r, columns, capacity))(
        routes_all.reshape(groups, slot_count)
    )
    token_of = jnp.minimum(slot_of_all // top_count, local_tokens - 1)
    token_of = token_of.reshape(groups, columns, capacity).transpose(1, 0, 2)
    flat_token = token_of + (jnp.arange(groups, dtype=jnp.int32) * local_tokens)[None, :, None]
    send_cot = cot_q.reshape(groups * local_tokens, quarter)[flat_token]
    got_cot = lax.all_to_all(send_cot, "expert", split_axis=0, concat_axis=0, tiled=True)

    clamped = jnp.minimum(slot_of, slot_count - 1)
    send_hidden = hidden.reshape(slot_count, hidden_width)[clamped].reshape(
        columns, capacity, hidden_width
    )
    send_gates = jnp.where(slot_of < slot_count, gates.reshape(slot_count)[clamped], 0.0).reshape(
        columns, capacity
    )
    got = lax.all_to_all(
        jnp.concatenate([send_hidden, split3(send_gates)], axis=2),
        "expert",
        split_axis=0,
        concat_axis=0,
        tiled=True,
    )
    got_hidden = got[:, :, :hidden_width]
    got_gates = join3(got[:, :, hidden_width:])

    scaled = (got_gates[:, :, None] * got_hidden.astype(jnp.float32)).astype(jnp.bfloat16)
    rows_all = lax.all_to_all(
        jnp.broadcast_to(scaled[None], (groups,) + scaled.shape),
        "dp",
        split_axis=0,
        concat_axis=0,
        tiled=True,
    )
    matrix = weight[0]
    partial_back = jnp.stack(
        [
            jnp.einsum("scd,fd->scf", got_cot[:, g], matrix, preferred_element_type=jnp.float32)
            for g in range(groups)
        ]
    )
    back = lax.psum_scatter(partial_back, "dp", scatter_dimension=0, tiled=True)[0]
    _, back = lax.optimization_barrier((rows_all, back))
    grad_matrix = jnp.einsum(
        "gscf,sgcd->fd", rows_all, got_cot, preferred_element_type=jnp.float32
    )
    grad_hidden_rows = (got_gates[:, :, None] * back).astype(jnp.bfloat16)
    grad_gates_rows = jnp.sum(got_hidden.astype(jnp.float32) * back, axis=2)
    payload = jnp.concatenate([grad_hidden_rows, split3(grad_gates_rows)], axis=2)
    grad_matrix, payload = lax.optimization_barrier((grad_matrix, payload))
    returned = lax.all_to_all(
        payload,
        "expert",
        split_axis=0,
        concat_axis=0,
        tiled=True,
    )
    returned_hidden = returned[:, :, :hidden_width]
    returned_gates = join3(returned[:, :, hidden_width:])
    grad_hidden = returned_hidden.reshape(columns * capacity, hidden_width)[destination].reshape(
        local_tokens, top_count, hidden_width
    )
    grad_gates = returned_gates.reshape(columns * capacity)[destination].reshape(
        local_tokens, top_count
    )
    return (grad_hidden, grad_gates, grad_matrix.astype(jnp.bfloat16)[None])


def solution(mesh):
    placed = (
        P(("dp", "expert"), None, None),
        P(("dp", "expert"), None),
        P(("dp", "expert"), None),
        P(("dp", "expert"), None),
        P("expert", None, "dp"),
    )
    return jax.shard_map(
        per_device,
        mesh=mesh,
        in_specs=placed,
        out_specs=(
            P(("dp", "expert"), None, None),
            P(("dp", "expert"), None),
            P("expert", None, "dp"),
        ),
        check_vma=False,
    )
```

```python
import jax
import jax.numpy as jnp
from jax import lax
from jax.sharding import PartitionSpec as P


def slots_for(flat_experts, columns, capacity):
    slot_count = flat_experts.shape[0]
    one_hot = (flat_experts[:, None] == jnp.arange(columns, dtype=jnp.int32)[None, :]).astype(
        jnp.int32
    )
    earlier = jnp.cumsum(one_hot, axis=0) - one_hot
    position = jnp.sum(earlier * one_hot, axis=1)
    destination = flat_experts * capacity + position
    slot_of = (
        jnp.full((columns * capacity,), slot_count, jnp.int32)
        .at[destination]
        .set(jnp.arange(slot_count, dtype=jnp.int32))
    )
    return destination, slot_of


LANES = 128


def split3(values):
    pieces = []
    rest = values
    for _ in range(3):
        head = lax.reduce_precision(rest, exponent_bits=8, mantissa_bits=7)
        pieces.append(head.astype(jnp.bfloat16))
        rest = rest - head
    pad = jnp.zeros(values.shape + (LANES - 3,), jnp.bfloat16)
    return jnp.concatenate([jnp.stack(pieces, axis=-1), pad], axis=-1)


def join3(lanes):
    pieces = lanes[..., :3].astype(jnp.float32)
    return (pieces[..., 0] + pieces[..., 1]) + pieces[..., 2]


def per_device(hidden, routes, gates, cotangent, weight):
    local_tokens, top_count, hidden_width = hidden.shape
    columns = lax.axis_size("expert")
    groups = lax.axis_size("dp")
    capacity = min(local_tokens, 2 * local_tokens * top_count // columns)
    slot_count = local_tokens * top_count
    quarter = cotangent.shape[1] // groups

    routes_all = lax.all_gather(routes.reshape(slot_count), "dp", axis=0, tiled=False)
    _, slot_of_all = jax.vmap(lambda r: slots_for(r, columns, capacity))(routes_all)
    destination, slot_of = slots_for(routes.reshape(slot_count), columns, capacity)

    cot_split = cotangent.reshape(local_tokens, groups, quarter).transpose(1, 0, 2)
    cot_q = lax.all_to_all(cot_split, "dp", split_axis=0, concat_axis=0, tiled=True)
    token_of = jnp.minimum(slot_of_all // top_count, local_tokens - 1)
    token_of = token_of.reshape(groups, columns, capacity).transpose(1, 0, 2)
    flat_token = token_of + (jnp.arange(groups, dtype=jnp.int32) * local_tokens)[None, :, None]
    send_cot = cot_q.reshape(groups * local_tokens, quarter)[flat_token]
    got_cot = lax.all_to_all(send_cot, "expert", split_axis=0, concat_axis=0, tiled=True)

    clamped = jnp.minimum(slot_of, slot_count - 1)
    send_hidden = hidden.reshape(slot_count, hidden_width)[clamped].reshape(
        columns, capacity, hidden_width
    )
    send_gates = jnp.where(slot_of < slot_count, gates.reshape(slot_count)[clamped], 0.0).reshape(
        columns, capacity
    )
    got = lax.all_to_all(
        jnp.concatenate([send_hidden, split3(send_gates)], axis=2),
        "expert",
        split_axis=0,
        concat_axis=0,
        tiled=True,
    )
    got_hidden = got[:, :, :hidden_width]
    got_gates = join3(got[:, :, hidden_width:])

    scaled = (got_gates[:, :, None] * got_hidden.astype(jnp.float32)).astype(jnp.bfloat16)
    rows_all = lax.all_gather(scaled, "dp", axis=0, tiled=False)
    matrix = weight[0]
    partial_back = jnp.stack(
        [
            jnp.einsum("scd,fd->scf", got_cot[:, g], matrix, preferred_element_type=jnp.float32)
            for g in range(groups)
        ]
    )
    back = lax.psum_scatter(partial_back, "dp", scatter_dimension=0, tiled=True)[0]
    grad_matrix = jnp.einsum(
        "gscf,sgcd->fd", rows_all, got_cot, preferred_element_type=jnp.float32
    )
    grad_hidden_rows = (got_gates[:, :, None] * back).astype(jnp.bfloat16)
    grad_gates_rows = jnp.sum(got_hidden.astype(jnp.float32) * back, axis=2)
    returned = lax.all_to_all(
        jnp.concatenate([grad_hidden_rows, split3(grad_gates_rows)], axis=2),
        "expert",
        split_axis=0,
        concat_axis=0,
        tiled=True,
    )
    returned_hidden = returned[:, :, :hidden_width]
    returned_gates = join3(returned[:, :, hidden_width:])
    grad_hidden = returned_hidden.reshape(columns * capacity, hidden_width)[destination].reshape(
        local_tokens, top_count, hidden_width
    )
    grad_gates = returned_gates.reshape(columns * capacity)[destination].reshape(
        local_tokens, top_count
    )
    return (grad_hidden, grad_gates, grad_matrix.astype(jnp.bfloat16)[None])


def solution(mesh):
    placed = (
        P(("dp", "expert"), None, None),
        P(("dp", "expert"), None),
        P(("dp", "expert"), None),
        P(("dp", "expert"), None),
        P("expert", None, "dp"),
    )
    return jax.shard_map(
        per_device,
        mesh=mesh,
        in_specs=placed,
        out_specs=(
            P(("dp", "expert"), None, None),
            P(("dp", "expert"), None),
            P("expert", None, "dp"),
        ),
        check_vma=False,
    )
```

```python
import jax
import jax.numpy as jnp
from jax import lax
from jax.sharding import PartitionSpec as P


def slots_for(flat_experts, columns, capacity):
    slot_count = flat_experts.shape[0]
    one_hot = (flat_experts[:, None] == jnp.arange(columns, dtype=jnp.int32)[None, :]).astype(
        jnp.int32
    )
    earlier = jnp.cumsum(one_hot, axis=0) - one_hot
    position = jnp.sum(earlier * one_hot, axis=1)
    destination = flat_experts * capacity + position
    slot_of = (
        jnp.full((columns * capacity,), slot_count, jnp.int32)
        .at[destination]
        .set(jnp.arange(slot_count, dtype=jnp.int32))
    )
    return destination, slot_of


LANES = 128


def split3(values):
    pieces = []
    rest = values
    for _ in range(3):
        head = lax.reduce_precision(rest, exponent_bits=8, mantissa_bits=7)
        pieces.append(head.astype(jnp.bfloat16))
        rest = rest - head
    pad = jnp.zeros(values.shape + (LANES - 3,), jnp.bfloat16)
    return jnp.concatenate([jnp.stack(pieces, axis=-1), pad], axis=-1)


def join3(lanes):
    pieces = lanes[..., :3].astype(jnp.float32)
    return (pieces[..., 0] + pieces[..., 1]) + pieces[..., 2]


def per_device(hidden, routes, gates, cotangent, weight):
    local_tokens, top_count, hidden_width = hidden.shape
    columns = lax.axis_size("expert")
    groups = lax.axis_size("dp")
    capacity = min(local_tokens, 2 * local_tokens * top_count // columns)
    slot_count = local_tokens * top_count
    quarter = cotangent.shape[1] // groups

    routes_all = lax.all_to_all(
        jnp.broadcast_to(routes.reshape(1, slot_count), (groups, slot_count)),
        "dp",
        split_axis=0,
        concat_axis=0,
        tiled=True,
    )
    _, slot_of_all = jax.vmap(lambda r: slots_for(r, columns, capacity))(routes_all)
    destination, slot_of = slots_for(routes.reshape(slot_count), columns, capacity)

    cot_split = cotangent.reshape(local_tokens, groups, quarter).transpose(1, 0, 2)
    cot_q = lax.all_to_all(cot_split, "dp", split_axis=0, concat_axis=0, tiled=True)
    token_of = jnp.minimum(slot_of_all // top_count, local_tokens - 1)
    token_of = token_of.reshape(groups, columns, capacity).transpose(1, 0, 2)
    flat_token = token_of + (jnp.arange(groups, dtype=jnp.int32) * local_tokens)[None, :, None]
    send_cot = cot_q.reshape(groups * local_tokens, quarter)[flat_token]
    got_cot = lax.all_to_all(send_cot, "expert", split_axis=0, concat_axis=0, tiled=True)

    clamped = jnp.minimum(slot_of, slot_count - 1)
    send_hidden = hidden.reshape(slot_count, hidden_width)[clamped].reshape(
        columns, capacity, hidden_width
    )
    send_gates = jnp.where(slot_of < slot_count, gates.reshape(slot_count)[clamped], 0.0).reshape(
        columns, capacity
    )
    got = lax.all_to_all(
        jnp.concatenate([send_hidden, split3(send_gates)], axis=2),
        "expert",
        split_axis=0,
        concat_axis=0,
        tiled=True,
    )
    got_hidden = got[:, :, :hidden_width]
    got_gates = join3(got[:, :, hidden_width:])

    scaled = (got_gates[:, :, None] * got_hidden.astype(jnp.float32)).astype(jnp.bfloat16)
    rows_all = lax.all_gather(scaled, "dp", axis=0, tiled=False)
    matrix = weight[0]
    partial_back = jnp.stack(
        [
            jnp.einsum("scd,fd->scf", got_cot[:, g], matrix, preferred_element_type=jnp.float32)
            for g in range(groups)
        ]
    )
    back = lax.psum_scatter(partial_back, "dp", scatter_dimension=0, tiled=True)[0]
    grad_matrix = jnp.einsum(
        "gscf,sgcd->fd", rows_all, got_cot, preferred_element_type=jnp.float32
    )
    grad_hidden_rows = (got_gates[:, :, None] * back).astype(jnp.bfloat16)
    grad_gates_rows = jnp.sum(got_hidden.astype(jnp.float32) * back, axis=2)
    returned = lax.all_to_all(
        jnp.concatenate([grad_hidden_rows, split3(grad_gates_rows)], axis=2),
        "expert",
        split_axis=0,
        concat_axis=0,
        tiled=True,
    )
    returned_hidden = returned[:, :, :hidden_width]
    returned_gates = join3(returned[:, :, hidden_width:])
    grad_hidden = returned_hidden.reshape(columns * capacity, hidden_width)[destination].reshape(
        local_tokens, top_count, hidden_width
    )
    grad_gates = returned_gates.reshape(columns * capacity)[destination].reshape(
        local_tokens, top_count
    )
    return (grad_hidden, grad_gates, grad_matrix.astype(jnp.bfloat16)[None])


def solution(mesh):
    placed = (
        P(("dp", "expert"), None, None),
        P(("dp", "expert"), None),
        P(("dp", "expert"), None),
        P(("dp", "expert"), None),
        P("expert", None, "dp"),
    )
    return jax.shard_map(
        per_device,
        mesh=mesh,
        in_specs=placed,
        out_specs=(
            P(("dp", "expert"), None, None),
            P(("dp", "expert"), None),
            P("expert", None, "dp"),
        ),
        check_vma=False,
    )
```
